128 devices in a mesh: chan: 16 (over y_lo, z, core), hour: 8 (over y_hi, x).
Axes of the slice: x: 4, y: 4 (y_hi: 2, y_lo: 2; y = y_hi * 2 + y_lo), z: 4, core: 2. Of those that a mesh axis runs over, the one named last changes fastest.
Arguments:
- spectra: bfloat16 [64, 128, 4096], P('hour', 'chan'), may hold values from -200 to 200
- quality: int32 [128], P('chan'), may hold values 0 or 1
- plan: int32 [4], replicated, may hold values from 1 to 15, as said below
Outputs:
- correlations: float32 [4, 8, 128, 512], P(None, 'hour', 'chan')
The draws below stay inside these ranges and needn't reach their ends.
Inputs may be any that keep to these rules, and one draw needn't show every extreme that they name: `plan`: distinct numbers; 1 and 15 are among them.
All inputs are finite; a program needn't handle non-finite values. No bound on the sum of `quality` on one device may be relied on, other than what follows from the above.
Results may differ from the reference program's by a relative error of at most 0.004.
Values may be sent and summed in bfloat16 or wider, within the bound.
No kernel may reach another device: no remote copies, remote signals or barrier semaphores. Data moves between devices by JAX's collectives and lax.ppermute only.
A program may use at most 320 MiB of HBM per device.

```python
import math
import jax
import jax.numpy as jnp
from jax import lax

FREQS = 2048
BAND = 64
LAGS = 512
ROUNDS = 4
C_DEV = 8
CHANNELS = 128
HOURS = 64
N_CHAN = 16


def draw_spectra(key, part):
    keys = jax.random.split(key, 3)
    shape = (HOURS, CHANNELS, 2 * FREQS)
    base = jnp.clip(jax.random.normal(keys[0], shape, jnp.float32), -6.0, 6.0)
    row_scale = jnp.exp(jax.random.uniform(keys[1], (HOURS, CHANNELS, 1), jnp.float32) * math.log(10.0))
    col_half = jnp.exp(jax.random.uniform(keys[2], (1, 1, FREQS), jnp.float32) * math.log(10.0))
    col_scale = jnp.concatenate([col_half, col_half], axis=-1)
    return (base * row_scale * col_scale * 0.3).astype(jnp.bfloat16)


def draw_plan(key, part):
    others = jax.random.permutation(key, N_CHAN - 3)[:ROUNDS - 2].astype(jnp.int32) + 2
    values = jnp.concatenate([jnp.array([N_CHAN - 1, 1], dtype=jnp.int32), others])
    order = jax.random.permutation(jax.random.fold_in(key, 7), ROUNDS)
    return values[order]


def touch_ends(entries, own_key, smallest, top_value):
    longest = entries.shape.index(max(entries.shape))
    spots = []
    for shift in (0, 1):
        where = [jax.random.randint(jax.random.fold_in(own_key, axis), (), 0, length) for axis, length in enumerate(entries.shape)]
        where[longest] = (where[longest] + shift) % entries.shape[longest]
        spots.append(tuple(where))
    return entries.at[spots[0]].set(smallest).at[spots[1]].set(top_value)


def setup_inputs(seed: int = 0) -> dict:
    splits = jax.random.split(jax.random.key(seed), 4)
    return {
        "spectra": draw_spectra(jax.random.fold_in(splits[3], 71), 0),
        "quality": touch_ends((jax.random.randint(splits[1], (CHANNELS,), 0, 4) < 3).astype(jnp.int32), jax.random.fold_in(splits[1], 1), 0, 1),
        "plan": draw_plan(jax.random.fold_in(splits[3], 71), 0),
    }


def whiten(spectra, quality):
    hours, chans, width = spectra.shape
    n_freq = width // 2
    values = spectra.astype(jnp.float32)
    real_part = values[..., :n_freq]
    imag_part = values[..., n_freq:]
    power_sum = real_part * real_part + imag_part * imag_part
    band_mean = lax.optimization_barrier(jnp.mean(power_sum.reshape(hours, chans, n_freq // BAND, BAND), axis=-1, keepdims=True))
    gain_band = lax.rsqrt(band_mean + 1e-06)
    gain_full = jnp.broadcast_to(gain_band, (hours, chans, n_freq // BAND, BAND)).reshape(hours, chans, n_freq)
    gain_both = jnp.concatenate([gain_full, gain_full], axis=-1)
    scaled = values * gain_both * quality.astype(jnp.float32)[None, :, None]
    return scaled.astype(jnp.bfloat16)

def lag_table(n_freq, total_hours):
    freq_index = jnp.arange(n_freq, dtype=jnp.int32)[:, None]
    lag_index = jnp.arange(LAGS, dtype=jnp.int32)[None, :] - LAGS // 2
    phase_int = freq_index * lag_index % (2 * n_freq)
    angle = jnp.pi * phase_int.astype(jnp.float32) / n_freq
    factor = 1.0 / jnp.sqrt(jnp.float32(total_hours * n_freq))
    return jnp.concatenate([jnp.cos(angle), -jnp.sin(angle)], axis=0) * factor

def reference(spectra, quality, plan):
    whitened = whiten(spectra, quality).astype(jnp.float32)
    n_freq = FREQS
    blocks = whitened.reshape(HOURS, N_CHAN, C_DEV, 2 * n_freq)
    own_re = blocks[..., :n_freq]
    own_im = blocks[..., n_freq:]
    weights = lag_table(n_freq, HOURS)
    hp = lax.Precision.HIGHEST
    results = []
    for rnd_index in range(ROUNDS):
        partners = jnp.bitwise_xor(jnp.arange(N_CHAN, dtype=jnp.int32), plan[rnd_index])
        partner = jnp.take(blocks, partners, axis=1)
        far_re = partner[..., :n_freq]
        far_im = partner[..., n_freq:]
        cross_re = jnp.einsum('hbjf,hbif->bjif', far_re, own_re, precision=hp) + jnp.einsum('hbjf,hbif->bjif', far_im, own_im, precision=hp)
        cross_im = jnp.einsum('hbjf,hbif->bjif', far_re, own_im, precision=hp) - jnp.einsum('hbjf,hbif->bjif', far_im, own_re, precision=hp)
        cross_spec = jnp.concatenate([cross_re, cross_im], axis=-1)
        flat = cross_spec.reshape(N_CHAN * C_DEV * C_DEV, 2 * n_freq)
        lagged = jnp.dot(flat, weights, precision=hp, preferred_element_type=jnp.float32)
        lagged = lagged.reshape(N_CHAN, C_DEV, C_DEV, LAGS).transpose(1, 0, 2, 3).reshape(C_DEV, N_CHAN * C_DEV, LAGS)
        results.append(lagged)
    return jnp.stack(results)
```

```python
import jax
import jax.numpy as jnp
from jax import lax
from jax.sharding import PartitionSpec as P

BAND = 64
LAGS = 512
ROUNDS = 4


def xor_permute(value, axis, mask):
    return lax.ppermute(value, axis, [(i, i ^ mask) for i in range(lax.axis_size(axis))])


def whiten(spectra, quality):
    hours, chans, width = spectra.shape
    n_freq = width // 2
    values = spectra.astype(jnp.float32)
    real_part = values[..., :n_freq]
    imag_part = values[..., n_freq:]
    power_sum = real_part * real_part + imag_part * imag_part
    band_mean = jnp.mean(
        power_sum.reshape(hours, chans, n_freq // BAND, BAND), axis=-1, keepdims=True
    )
    gain_band = lax.rsqrt(band_mean + 1e-06)
    gain_full = jnp.broadcast_to(gain_band, (hours, chans, n_freq // BAND, BAND)).reshape(
        hours, chans, n_freq
    )
    gain_both = jnp.concatenate([gain_full, gain_full], axis=-1)
    scaled = values * gain_both * quality.astype(jnp.float32)[None, :, None]
    return scaled.astype(jnp.bfloat16)


def lag_table(n_freq, total_hours):
    period = 2 * n_freq
    fine_n = 64
    lag_index = jnp.arange(LAGS, dtype=jnp.int32)[None, :] - LAGS // 2

    def angles(freqs):
        phase_int = freqs[:, None] * lag_index % period
        return jnp.pi * phase_int.astype(jnp.float32) / n_freq

    hi = angles(jnp.arange(n_freq // fine_n, dtype=jnp.int32) * fine_n)
    lo = angles(jnp.arange(fine_n, dtype=jnp.int32))
    cos_hi, sin_hi = jnp.cos(hi)[:, None, :], jnp.sin(hi)[:, None, :]
    cos_lo, sin_lo = jnp.cos(lo)[None, :, :], jnp.sin(lo)[None, :, :]
    factor = 1.0 / jnp.sqrt(jnp.float32(total_hours * n_freq))
    cos_t = (cos_hi * cos_lo - sin_hi * sin_lo).reshape(n_freq, LAGS) * factor
    neg_sin_t = (-(sin_hi * cos_lo + cos_hi * sin_lo)).reshape(n_freq, LAGS) * factor
    return cos_t, neg_sin_t


def cross_spectrum(own_block, partner):
    n_freq = own_block.shape[2] // 2
    a = own_block.astype(jnp.float32)
    b = partner.astype(jnp.float32)
    a_re = a[:, None, :, :n_freq]
    a_im = a[:, None, :, n_freq:]
    b_re = b[:, :, None, :n_freq]
    b_im = b[:, :, None, n_freq:]
    cross_re = jnp.sum(b_re * a_re + b_im * a_im, axis=0)
    cross_im = jnp.sum(b_re * a_im - b_im * a_re, axis=0)
    return cross_re, cross_im


def per_device(spectra, quality, plan):
    hours, chans, width = spectra.shape
    n_freq = width // 2
    n_chan = lax.axis_size("chan")
    n_hour = lax.axis_size("hour")
    own_block = whiten(spectra, quality)
    cos_t, neg_sin_t = lag_table(n_freq, hours * n_hour)

    others = (plan != 1) & (plan != n_chan - 1)
    first = jnp.argmax(others).astype(jnp.int32)
    last = (ROUNDS - 1 - jnp.argmax(others[::-1])).astype(jnp.int32)
    branches = [
        (lambda v, m=m: xor_permute(v, "chan", m)) for m in range(1, n_chan)
    ]
    partners = [
        xor_permute(own_block, "chan", 1),
        xor_permute(own_block, "chan", n_chan - 1),
        lax.switch(plan[first] - 1, branches, own_block),
        lax.switch(plan[last] - 1, branches, own_block),
    ]
    re_parts, im_parts = [], []
    for partner in partners:
        cross_re, cross_im = cross_spectrum(own_block, partner)
        re_parts.append(cross_re)
        im_parts.append(cross_im)
    cross_re = jnp.stack(re_parts, axis=1).reshape(-1, n_freq)
    cross_im = jnp.stack(im_parts, axis=1).reshape(-1, n_freq)
    hp = lax.Precision.HIGHEST
    lagged = jnp.dot(cross_re, cos_t, precision=hp, preferred_element_type=jnp.float32)
    lagged = lagged + jnp.dot(
        cross_im, neg_sin_t, precision=hp, preferred_element_type=jnp.float32
    )
    lagged = lagged.reshape(chans, ROUNDS * chans, LAGS)

    me = lax.axis_index("hour")
    total = lax.dynamic_index_in_dim(lagged, me, axis=0, keepdims=False)
    for dist in range(1, n_hour):
        piece = lax.dynamic_index_in_dim(lagged, me ^ dist, axis=0, keepdims=False)
        total = total + xor_permute(piece, "hour", dist)
    total = total.reshape(ROUNDS, chans, LAGS)

    slot = jnp.where(
        plan == 1,
        0,
        jnp.where(
            plan == n_chan - 1,
            1,
            jnp.where(jnp.arange(ROUNDS, dtype=jnp.int32) == first, 2, 3),
        ),
    ).astype(jnp.int32)
    result = jnp.take(total, slot, axis=0)
    return result[:, None]


def solution(mesh):
    return jax.shard_map(
        per_device,
        mesh=mesh,
        in_specs=(P("hour", "chan", None), P("chan"), P()),
        out_specs=P(None, "hour", "chan", None),
        check_vma=False,
    )
```

```python
import jax
import jax.numpy as jnp
from jax import lax
from jax.sharding import PartitionSpec as P

BAND = 64
LAGS = 512
ROUNDS = 4


def xor_permute(value, axis, mask):
    return lax.ppermute(value, axis, [(i, i ^ mask) for i in range(lax.axis_size(axis))])


def whiten(spectra, quality):
    hours, chans, width = spectra.shape
    n_freq = width // 2
    values = spectra.astype(jnp.float32)
    real_part = values[..., :n_freq]
    imag_part = values[..., n_freq:]
    power_sum = real_part * real_part + imag_part * imag_part
    band_mean = jnp.mean(
        power_sum.reshape(hours, chans, n_freq // BAND, BAND), axis=-1, keepdims=True
    )
    gain_band = lax.rsqrt(band_mean + 1e-06)
    gain_full = jnp.broadcast_to(gain_band, (hours, chans, n_freq // BAND, BAND)).reshape(
        hours, chans, n_freq
    )
    gain_both = jnp.concatenate([gain_full, gain_full], axis=-1)
    scaled = values * gain_both * quality.astype(jnp.float32)[None, :, None]
    return scaled.astype(jnp.bfloat16)


def lag_table(n_freq, total_hours):
    period = 2 * n_freq
    fine_n = 64
    lag_index = jnp.arange(LAGS, dtype=jnp.int32)[None, :] - LAGS // 2

    def angles(freqs):
        phase_int = freqs[:, None] * lag_index % period
        return jnp.pi * phase_int.astype(jnp.float32) / n_freq

    hi = angles(jnp.arange(n_freq // fine_n, dtype=jnp.int32) * fine_n)
    lo = angles(jnp.arange(fine_n, dtype=jnp.int32))
    cos_hi, sin_hi = jnp.cos(hi)[:, None, :], jnp.sin(hi)[:, None, :]
    cos_lo, sin_lo = jnp.cos(lo)[None, :, :], jnp.sin(lo)[None, :, :]
    factor = 1.0 / jnp.sqrt(jnp.float32(total_hours * n_freq))
    cos_t = (cos_hi * cos_lo - sin_hi * sin_lo).reshape(n_freq, LAGS) * factor
    neg_sin_t = (-(sin_hi * cos_lo + cos_hi * sin_lo)).reshape(n_freq, LAGS) * factor
    return cos_t, neg_sin_t


def cross_spectrum(own_block, partner):
    n_freq = own_block.shape[2] // 2
    a = own_block.astype(jnp.float32)
    b = partner.astype(jnp.float32)
    a_re = a[:, None, :, :n_freq]
    a_im = a[:, None, :, n_freq:]
    b_re = b[:, :, None, :n_freq]
    b_im = b[:, :, None, n_freq:]
    cross_re = jnp.sum(b_re * a_re + b_im * a_im, axis=0)
    cross_im = jnp.sum(b_re * a_im - b_im * a_re, axis=0)
    return cross_re, cross_im


def per_device(spectra, quality, plan):
    hours, chans, width = spectra.shape
    n_freq = width // 2
    n_chan = lax.axis_size("chan")
    n_hour = lax.axis_size("hour")
    own_block = whiten(spectra, quality)
    cos_t, neg_sin_t = lag_table(n_freq, hours * n_hour)

    others = (plan != 1) & (plan != n_chan - 1)
    first = jnp.argmax(others).astype(jnp.int32)
    last = (ROUNDS - 1 - jnp.argmax(others[::-1])).astype(jnp.int32)
    branches = [
        (lambda v, m=m: xor_permute(v, "chan", m)) for m in range(1, n_chan)
    ]
    partners = [
        xor_permute(own_block, "chan", 1),
        xor_permute(own_block, "chan", n_chan - 1),
        lax.switch(plan[first] - 1, branches, own_block),
        lax.switch(plan[last] - 1, branches, own_block),
    ]
    re_parts, im_parts = [], []
    for partner in partners:
        cross_re, cross_im = cross_spectrum(own_block, partner)
        re_parts.append(cross_re)
        im_parts.append(cross_im)
    cross_re = jnp.stack(re_parts, axis=1).reshape(-1, n_freq)
    cross_im = jnp.stack(im_parts, axis=1).reshape(-1, n_freq)
    hp = lax.Precision.HIGHEST
    lagged = jnp.dot(cross_re, cos_t, precision=hp, preferred_element_type=jnp.float32)
    lagged = lagged + jnp.dot(
        cross_im, neg_sin_t, precision=hp, preferred_element_type=jnp.float32
    )
    lagged = lagged.reshape(chans, ROUNDS * chans, LAGS)

    gathered = lax.all_to_all(lagged, "hour", 0, 0, tiled=True)
    total = jnp.sum(gathered, axis=0).reshape(ROUNDS, chans, LAGS)

    slot = jnp.where(
        plan == 1,
        0,
        jnp.where(
            plan == n_chan - 1,
            1,
            jnp.where(jnp.arange(ROUNDS, dtype=jnp.int32) == first, 2, 3),
        ),
    ).astype(jnp.int32)
    result = jnp.take(total, slot, axis=0)
    return result[:, None]


def solution(mesh):
    return jax.shard_map(
        per_device,
        mesh=mesh,
        in_specs=(P("hour", "chan", None), P("chan"), P()),
        out_specs=P(None, "hour", "chan", None),
        check_vma=False,
    )
```

```python
import jax
import jax.numpy as jnp
from jax import lax
from jax.sharding import PartitionSpec as P

BAND = 64
LAGS = 512
ROUNDS = 4


def xor_permute(value, axis, mask):
    return lax.ppermute(value, axis, [(i, i ^ mask) for i in range(lax.axis_size(axis))])


def whiten(spectra, quality):
    hours, chans, width = spectra.shape
    n_freq = width // 2
    values = spectra.astype(jnp.float32)
    real_part = values[..., :n_freq]
    imag_part = values[..., n_freq:]
    power_sum = real_part * real_part + imag_part * imag_part
    band_mean = jnp.mean(
        power_sum.reshape(hours, chans, n_freq // BAND, BAND), axis=-1, keepdims=True
    )
    gain_band = lax.rsqrt(band_mean + 1e-06)
    gain_full = jnp.broadcast_to(gain_band, (hours, chans, n_freq // BAND, BAND)).reshape(
        hours, chans, n_freq
    )
    gain_both = jnp.concatenate([gain_full, gain_full], axis=-1)
    scaled = values * gain_both * quality.astype(jnp.float32)[None, :, None]
    return scaled.astype(jnp.bfloat16)


def lag_table(n_freq, total_hours):
    period = 2 * n_freq
    fine_n = 64
    lag_index = jnp.arange(LAGS, dtype=jnp.int32)[None, :] - LAGS // 2

    def angles(freqs):
        phase_int = freqs[:, None] * lag_index % period
        return jnp.pi * phase_int.astype(jnp.float32) / n_freq

    hi = angles(jnp.arange(n_freq // fine_n, dtype=jnp.int32) * fine_n)
    lo = angles(jnp.arange(fine_n, dtype=jnp.int32))
    cos_hi, sin_hi = jnp.cos(hi)[:, None, :], jnp.sin(hi)[:, None, :]
    cos_lo, sin_lo = jnp.cos(lo)[None, :, :], jnp.sin(lo)[None, :, :]
    factor = 1.0 / jnp.sqrt(jnp.float32(total_hours * n_freq))
    cos_t = (cos_hi * cos_lo - sin_hi * sin_lo).reshape(n_freq, LAGS) * factor
    neg_sin_t = (-(sin_hi * cos_lo + cos_hi * sin_lo)).reshape(n_freq, LAGS) * factor
    return cos_t, neg_sin_t


def cross_spectrum(own_block, partner):
    n_freq = own_block.shape[2] // 2
    a = own_block.astype(jnp.float32)
    b = partner.astype(jnp.float32)
    a_re = a[:, None, :, :n_freq]
    a_im = a[:, None, :, n_freq:]
    b_re = b[:, :, None, :n_freq]
    b_im = b[:, :, None, n_freq:]
    cross_re = jnp.sum(b_re * a_re + b_im * a_im, axis=0)
    cross_im = jnp.sum(b_re * a_im - b_im * a_re, axis=0)
    return cross_re, cross_im


def per_device(spectra, quality, plan):
    hours, chans, width = spectra.shape
    n_freq = width // 2
    n_chan = lax.axis_size("chan")
    n_hour = lax.axis_size("hour")
    own_block = whiten(spectra, quality)
    cos_t, neg_sin_t = lag_table(n_freq, hours * n_hour)

    others = (plan != 1) & (plan != n_chan - 1)
    first = jnp.argmax(others).astype(jnp.int32)
    last = (ROUNDS - 1 - jnp.argmax(others[::-1])).astype(jnp.int32)
    branches = [
        (lambda v, m=m: xor_permute(v, "chan", m)) for m in range(1, n_chan)
    ]
    hp = lax.Precision.HIGHEST

    def lags_of(partners):
        re_parts, im_parts = [], []
        for partner in partners:
            cross_re, cross_im = cross_spectrum(own_block, partner)
            re_parts.append(cross_re)
            im_parts.append(cross_im)
        cross_re = jnp.stack(re_parts, axis=1).reshape(-1, n_freq)
        cross_im = jnp.stack(im_parts, axis=1).reshape(-1, n_freq)
        lagged = jnp.dot(cross_re, cos_t, precision=hp, preferred_element_type=jnp.float32)
        lagged = lagged + jnp.dot(
            cross_im, neg_sin_t, precision=hp, preferred_element_type=jnp.float32
        )
        return lagged.reshape(chans, len(partners) * chans, LAGS)

    def hour_sum(lagged):
        gathered = lax.all_to_all(lagged, "hour", 0, 0, tiled=True)
        return jnp.sum(gathered, axis=0)

    switched_a = lax.switch(plan[first] - 1, branches, own_block)
    next_block, _ = lax.optimization_barrier((own_block, switched_a))
    switched_b = lax.switch(plan[last] - 1, branches, next_block)
    late_block, _ = lax.optimization_barrier((own_block, switched_b))
    partners = [
        xor_permute(late_block, "chan", 1),
        xor_permute(late_block, "chan", n_chan - 1),
        switched_a,
        switched_b,
    ]
    lagged = lags_of(partners)
    total = hour_sum(lagged).reshape(ROUNDS, chans, LAGS)

    slot = jnp.where(
        plan == 1,
        0,
        jnp.where(
            plan == n_chan - 1,
            1,
            jnp.where(jnp.arange(ROUNDS, dtype=jnp.int32) == first, 2, 3),
        ),
    ).astype(jnp.int32)
    result = jnp.take(total, slot, axis=0)
    return result[:, None]


def solution(mesh):
    return jax.shard_map(
        per_device,
        mesh=mesh,
        in_specs=(P("hour", "chan", None), P("chan"), P()),
        out_specs=P(None, "hour", "chan", None),
        check_vma=False,
    )
```

```python
import jax
import jax.numpy as jnp
from jax import lax
from jax.sharding import PartitionSpec as P

BAND = 64
LAGS = 512
ROUNDS = 4


def xor_permute(value, axis, mask):
    return lax.ppermute(value, axis, [(i, i ^ mask) for i in range(lax.axis_size(axis))])


def whiten(spectra, quality):
    hours, chans, width = spectra.shape
    n_freq = width // 2
    values = spectra.astype(jnp.float32)
    real_part = values[..., :n_freq]
    imag_part = values[..., n_freq:]
    power_sum = real_part * real_part + imag_part * imag_part
    band_mean = jnp.mean(
        power_sum.reshape(hours, chans, n_freq // BAND, BAND), axis=-1, keepdims=True
    )
    gain_band = lax.rsqrt(band_mean + 1e-06)
    gain_full = jnp.broadcast_to(gain_band, (hours, chans, n_freq // BAND, BAND)).reshape(
        hours, chans, n_freq
    )
    gain_both = jnp.concatenate([gain_full, gain_full], axis=-1)
    scaled = values * gain_both * quality.astype(jnp.float32)[None, :, None]
    return scaled.astype(jnp.bfloat16)


def lag_table(n_freq, total_hours):
    period = 2 * n_freq
    fine_n = 64
    lag_index = jnp.arange(LAGS, dtype=jnp.int32)[None, :] - LAGS // 2

    def angles(freqs):
        phase_int = freqs[:, None] * lag_index % period
        return jnp.pi * phase_int.astype(jnp.float32) / n_freq

    hi = angles(jnp.arange(n_freq // fine_n, dtype=jnp.int32) * fine_n)
    lo = angles(jnp.arange(fine_n, dtype=jnp.int32))
    cos_hi, sin_hi = jnp.cos(hi)[:, None, :], jnp.sin(hi)[:, None, :]
    cos_lo, sin_lo = jnp.cos(lo)[None, :, :], jnp.sin(lo)[None, :, :]
    factor = 1.0 / jnp.sqrt(jnp.float32(total_hours * n_freq))
    cos_t = (cos_hi * cos_lo - sin_hi * sin_lo).reshape(n_freq, LAGS) * factor
    neg_sin_t = (-(sin_hi * cos_lo + cos_hi * sin_lo)).reshape(n_freq, LAGS) * factor
    return cos_t, neg_sin_t


def cross_spectrum(own_block, partner):
    n_freq = own_block.shape[2] // 2
    a = own_block.astype(jnp.float32)
    b = partner.astype(jnp.float32)
    a_re = a[:, None, :, :n_freq]
    a_im = a[:, None, :, n_freq:]
    b_re = b[:, :, None, :n_freq]
    b_im = b[:, :, None, n_freq:]
    cross_re = jnp.sum(b_re * a_re + b_im * a_im, axis=0)
    cross_im = jnp.sum(b_re * a_im - b_im * a_re, axis=0)
    return cross_re, cross_im


def per_device(spectra, quality, plan):
    hours, chans, width = spectra.shape
    n_freq = width // 2
    n_chan = lax.axis_size("chan")
    n_hour = lax.axis_size("hour")
    own_block = whiten(spectra, quality)
    cos_t, neg_sin_t = lag_table(n_freq, hours * n_hour)

    others = (plan != 1) & (plan != n_chan - 1)
    first = jnp.argmax(others).astype(jnp.int32)
    last = (ROUNDS - 1 - jnp.argmax(others[::-1])).astype(jnp.int32)
    branches = [
        (lambda v, m=m: xor_permute(v, "chan", m)) for m in range(1, n_chan)
    ]
    partners = [
        xor_permute(own_block, "chan", 1),
        xor_permute(own_block, "chan", n_chan - 1),
        lax.switch(plan[first] - 1, branches, own_block),
        lax.switch(plan[last] - 1, branches, own_block),
    ]
    re_parts, im_parts = [], []
    for partner in partners:
        cross_re, cross_im = cross_spectrum(own_block, partner)
        re_parts.append(cross_re)
        im_parts.append(cross_im)
    cross_re = jnp.stack(re_parts, axis=1).reshape(-1, n_freq)
    cross_im = jnp.stack(im_parts, axis=1).reshape(-1, n_freq)
    hp = lax.Precision.HIGH
    lagged = jnp.dot(cross_re, cos_t, precision=hp, preferred_element_type=jnp.float32)
    lagged = lagged + jnp.dot(
        cross_im, neg_sin_t, precision=hp, preferred_element_type=jnp.float32
    )
    lagged = lagged.reshape(chans, ROUNDS * chans, LAGS)

    gathered = lax.all_to_all(lagged, "hour", 0, 0, tiled=True)
    total = jnp.sum(gathered, axis=0).reshape(ROUNDS, chans, LAGS)

    slot = jnp.where(
        plan == 1,
        0,
        jnp.where(
            plan == n_chan - 1,
            1,
            jnp.where(jnp.arange(ROUNDS, dtype=jnp.int32) == first, 2, 3),
        ),
    ).astype(jnp.int32)
    result = jnp.take(total, slot, axis=0)
    return result[:, None]


def solution(mesh):
    return jax.shard_map(
        per_device,
        mesh=mesh,
        in_specs=(P("hour", "chan", None), P("chan"), P()),
        out_specs=P(None, "hour", "chan", None),
        check_vma=False,
    )
```

```python
import jax
import jax.numpy as jnp
from jax import lax
from jax.sharding import PartitionSpec as P

BAND = 64
LAGS = 512
ROUNDS = 4


def xor_permute(value, axis, mask):
    return lax.ppermute(value, axis, [(i, i ^ mask) for i in range(lax.axis_size(axis))])


def whiten(spectra, quality):
    hours, chans, width = spectra.shape
    n_freq = width // 2
    values = spectra.astype(jnp.float32)
    real_part = values[..., :n_freq]
    imag_part = values[..., n_freq:]
    power_sum = real_part * real_part + imag_part * imag_part
    band_mean = jnp.mean(
        power_sum.reshape(hours, chans, n_freq // BAND, BAND), axis=-1, keepdims=True
    )
    gain_band = lax.rsqrt(band_mean + 1e-06)
    gain_full = jnp.broadcast_to(gain_band, (hours, chans, n_freq // BAND, BAND)).reshape(
        hours, chans, n_freq
    )
    gain_both = jnp.concatenate([gain_full, gain_full], axis=-1)
    scaled = values * gain_both * quality.astype(jnp.float32)[None, :, None]
    return scaled.astype(jnp.bfloat16)


def lag_table(n_freq, total_hours):
    period = 2 * n_freq
    fine_n = 64
    lag_index = jnp.arange(LAGS, dtype=jnp.int32)[None, :] - LAGS // 2

    def angles(freqs):
        phase_int = freqs[:, None] * lag_index % period
        return jnp.pi * phase_int.astype(jnp.float32) / n_freq

    hi = angles(jnp.arange(n_freq // fine_n, dtype=jnp.int32) * fine_n)
    lo = angles(jnp.arange(fine_n, dtype=jnp.int32))
    cos_hi, sin_hi = jnp.cos(hi)[:, None, :], jnp.sin(hi)[:, None, :]
    cos_lo, sin_lo = jnp.cos(lo)[None, :, :], jnp.sin(lo)[None, :, :]
    factor = 1.0 / jnp.sqrt(jnp.float32(total_hours * n_freq))
    cos_t = (cos_hi * cos_lo - sin_hi * sin_lo).reshape(n_freq, LAGS) * factor
    neg_sin_t = (-(sin_hi * cos_lo + cos_hi * sin_lo)).reshape(n_freq, LAGS) * factor
    return cos_t, neg_sin_t


def cross_spectrum(own_block, partner):
    n_freq = own_block.shape[2] // 2
    a = own_block.astype(jnp.float32)
    b = partner.astype(jnp.float32)
    a_re = a[:, None, :, :n_freq]
    a_im = a[:, None, :, n_freq:]
    b_re = b[:, :, None, :n_freq]
    b_im = b[:, :, None, n_freq:]
    cross_re = jnp.sum(b_re * a_re + b_im * a_im, axis=0)
    cross_im = jnp.sum(b_re * a_im - b_im * a_re, axis=0)
    return cross_re, cross_im


def per_device(spectra, quality, plan):
    hours, chans, width = spectra.shape
    n_freq = width // 2
    n_chan = lax.axis_size("chan")
    n_hour = lax.axis_size("hour")
    own_block = whiten(spectra, quality)
    cos_t, neg_sin_t = lag_table(n_freq, hours * n_hour)

    others = (plan != 1) & (plan != n_chan - 1)
    low_mask = jnp.min(jnp.where(others, plan, n_chan))
    high_mask = jnp.max(jnp.where(others, plan, 0))
    branches = [
        (lambda v, m=m: xor_permute(v, "chan", m)) for m in range(1, n_chan)
    ]
    partners = [
        xor_permute(own_block, "chan", 1),
        xor_permute(own_block, "chan", n_chan - 1),
        lax.switch(low_mask - 1, branches, own_block),
        lax.switch(high_mask - 1, branches, own_block),
    ]
    re_parts, im_parts = [], []
    for partner in partners:
        cross_re, cross_im = cross_spectrum(own_block, partner)
        re_parts.append(cross_re)
        im_parts.append(cross_im)
    cross_re = jnp.stack(re_parts, axis=1).reshape(-1, n_freq)
    cross_im = jnp.stack(im_parts, axis=1).reshape(-1, n_freq)
    hp = lax.Precision.HIGH
    lagged = jnp.dot(cross_re, cos_t, precision=hp, preferred_element_type=jnp.float32)
    lagged = lagged + jnp.dot(
        cross_im, neg_sin_t, precision=hp, preferred_element_type=jnp.float32
    )
    lagged = lagged.reshape(chans, ROUNDS * chans, LAGS)

    gathered = lax.all_to_all(lagged, "hour", 0, 0, tiled=True)
    total = jnp.sum(gathered, axis=0).reshape(ROUNDS, chans, LAGS)

    slot = jnp.where(
        plan == 1,
        0,
        jnp.where(
            plan == n_chan - 1,
            1,
            jnp.where(plan == low_mask, 2, 3),
        ),
    ).astype(jnp.int32)
    result = jnp.take(total, slot, axis=0)
    return result[:, None]


def solution(mesh):
    return jax.shard_map(
        per_device,
        mesh=mesh,
        in_specs=(P("hour", "chan", None), P("chan"), P()),
        out_specs=P(None, "hour", "chan", None),
        check_vma=False,
    )
```

```python
import jax
import numpy as np
import jax.numpy as jnp
from jax import lax
from jax.sharding import PartitionSpec as P

BAND = 64
LAGS = 512
ROUNDS = 4


def xor_permute(value, axis, mask):
    return lax.ppermute(value, axis, [(i, i ^ mask) for i in range(lax.axis_size(axis))])


def whiten(spectra, quality):
    hours, chans, width = spectra.shape
    n_freq = width // 2
    values = spectra.astype(jnp.float32)
    real_part = values[..., :n_freq]
    imag_part = values[..., n_freq:]
    power_sum = real_part * real_part + imag_part * imag_part
    band_mean = jnp.mean(
        power_sum.reshape(hours, chans, n_freq // BAND, BAND), axis=-1, keepdims=True
    )
    gain_band = lax.rsqrt(band_mean + 1e-06)
    gain_full = jnp.broadcast_to(gain_band, (hours, chans, n_freq // BAND, BAND)).reshape(
        hours, chans, n_freq
    )
    gain_both = jnp.concatenate([gain_full, gain_full], axis=-1)
    scaled = values * gain_both * quality.astype(jnp.float32)[None, :, None]
    return scaled.astype(jnp.bfloat16)


def lag_table(n_freq, total_hours):
    period = 2 * n_freq
    fine_n = 64
    lag_index = jnp.arange(LAGS, dtype=jnp.int32)[None, :] - LAGS // 2

    def angles(freqs):
        phase_int = freqs[:, None] * lag_index % period
        return jnp.pi * phase_int.astype(jnp.float32) / n_freq

    hi = angles(jnp.arange(n_freq // fine_n, dtype=jnp.int32) * fine_n)
    lo = angles(jnp.arange(fine_n, dtype=jnp.int32))
    cos_hi, sin_hi = jnp.cos(hi)[:, None, :], jnp.sin(hi)[:, None, :]
    cos_lo, sin_lo = jnp.cos(lo)[None, :, :], jnp.sin(lo)[None, :, :]
    factor = 1.0 / jnp.sqrt(jnp.float32(total_hours * n_freq))
    cos_t = (cos_hi * cos_lo - sin_hi * sin_lo).reshape(n_freq, LAGS) * factor
    neg_sin_t = (-(sin_hi * cos_lo + cos_hi * sin_lo)).reshape(n_freq, LAGS) * factor
    return cos_t, neg_sin_t


def cross_spectrum(own_block, partner):
    n_freq = own_block.shape[2] // 2
    a = own_block.astype(jnp.float32)
    b = partner.astype(jnp.float32)
    a_re = a[:, None, :, :n_freq]
    a_im = a[:, None, :, n_freq:]
    b_re = b[:, :, None, :n_freq]
    b_im = b[:, :, None, n_freq:]
    cross_re = jnp.sum(b_re * a_re + b_im * a_im, axis=0)
    cross_im = jnp.sum(b_re * a_im - b_im * a_re, axis=0)
    return cross_re, cross_im


def per_device(spectra, quality, plan):
    hours, chans, width = spectra.shape
    n_freq = width // 2
    n_chan = lax.axis_size("chan")
    n_hour = lax.axis_size("hour")
    own_block = whiten(spectra, quality)
    cos_t, neg_sin_t = lag_table(n_freq, hours * n_hour)

    others = (plan != 1) & (plan != n_chan - 1)
    low_mask = jnp.min(jnp.where(others, plan, n_chan))
    high_mask = jnp.max(jnp.where(others, plan, 0))
    pairs = [(lo, hi) for lo in range(2, n_chan - 1) for hi in range(lo + 1, n_chan - 1)]
    pair_index = np.zeros((n_chan, n_chan), np.int32)
    for k, (lo, hi) in enumerate(pairs):
        pair_index[lo, hi] = k

    def fetch(block, lo, hi):
        return tuple(xor_permute(block, "chan", m) for m in (1, n_chan - 1, lo, hi))

    branches = [(lambda v, lo=lo, hi=hi: fetch(v, lo, hi)) for lo, hi in pairs]
    partners = lax.switch(jnp.asarray(pair_index)[low_mask, high_mask], branches, own_block)
    re_parts, im_parts = [], []
    for partner in partners:
        cross_re, cross_im = cross_spectrum(own_block, partner)
        re_parts.append(cross_re)
        im_parts.append(cross_im)
    cross_re = jnp.stack(re_parts, axis=1).reshape(-1, n_freq)
    cross_im = jnp.stack(im_parts, axis=1).reshape(-1, n_freq)
    hp = lax.Precision.HIGH
    lagged = jnp.dot(cross_re, cos_t, precision=hp, preferred_element_type=jnp.float32)
    lagged = lagged + jnp.dot(
        cross_im, neg_sin_t, precision=hp, preferred_element_type=jnp.float32
    )
    lagged = lagged.reshape(chans, ROUNDS * chans, LAGS)

    gathered = lax.all_to_all(lagged, "hour", 0, 0, tiled=True)
    total = jnp.sum(gathered, axis=0).reshape(ROUNDS, chans, LAGS)

    slot = jnp.where(
        plan == 1,
        0,
        jnp.where(
            plan == n_chan - 1,
            1,
            jnp.where(plan == low_mask, 2, 3),
        ),
    ).astype(jnp.int32)
    result = jnp.take(total, slot, axis=0)
    return result[:, None]


def solution(mesh):
    return jax.shard_map(
        per_device,
        mesh=mesh,
        in_specs=(P("hour", "chan", None), P("chan"), P()),
        out_specs=P(None, "hour", "chan", None),
        check_vma=False,
    )
```

```python
import jax
import jax.numpy as jnp
from jax import lax
from jax.sharding import PartitionSpec as P

BAND = 64
LAGS = 512
ROUNDS = 4


def xor_permute(value, axis, mask):
    return lax.ppermute(value, axis, [(i, i ^ mask) for i in range(lax.axis_size(axis))])


def whiten(spectra, quality):
    hours, chans, width = spectra.shape
    n_freq = width // 2
    values = spectra.astype(jnp.float32)
    real_part = values[..., :n_freq]
    imag_part = values[..., n_freq:]
    power_sum = real_part * real_part + imag_part * imag_part
    band_mean = jnp.mean(
        power_sum.reshape(hours, chans, n_freq // BAND, BAND), axis=-1, keepdims=True
    )
    gain_band = lax.rsqrt(band_mean + 1e-06)
    gain_full = jnp.broadcast_to(gain_band, (hours, chans, n_freq // BAND, BAND)).reshape(
        hours, chans, n_freq
    )
    gain_both = jnp.concatenate([gain_full, gain_full], axis=-1)
    scaled = values * gain_both * quality.astype(jnp.float32)[None, :, None]
    return scaled.astype(jnp.bfloat16)


def lag_table(n_freq, total_hours):
    period = 2 * n_freq
    fine_n = 64
    lag_index = jnp.arange(LAGS, dtype=jnp.int32)[None, :] - LAGS // 2

    def angles(freqs):
        phase_int = freqs[:, None] * lag_index % period
        return jnp.pi * phase_int.astype(jnp.float32) / n_freq

    hi = angles(jnp.arange(n_freq // fine_n, dtype=jnp.int32) * fine_n)
    lo = angles(jnp.arange(fine_n, dtype=jnp.int32))
    cos_hi, sin_hi = jnp.cos(hi)[:, None, :], jnp.sin(hi)[:, None, :]
    cos_lo, sin_lo = jnp.cos(lo)[None, :, :], jnp.sin(lo)[None, :, :]
    factor = 1.0 / jnp.sqrt(jnp.float32(total_hours * n_freq))
    cos_t = (cos_hi * cos_lo - sin_hi * sin_lo).reshape(n_freq, LAGS) * factor
    neg_sin_t = (-(sin_hi * cos_lo + cos_hi * sin_lo)).reshape(n_freq, LAGS) * factor
    return cos_t, neg_sin_t


def cross_spectrum(own_block, partner):
    n_freq = own_block.shape[2] // 2
    a = own_block.astype(jnp.float32)
    b = partner.astype(jnp.float32)
    a_re = a[:, None, :, :n_freq]
    a_im = a[:, None, :, n_freq:]
    b_re = b[:, :, None, :n_freq]
    b_im = b[:, :, None, n_freq:]
    cross_re = jnp.sum(b_re * a_re + b_im * a_im, axis=0)
    cross_im = jnp.sum(b_re * a_im - b_im * a_re, axis=0)
    return cross_re, cross_im


def per_device(spectra, quality, plan):
    hours, chans, width = spectra.shape
    n_freq = width // 2
    n_chan = lax.axis_size("chan")
    n_hour = lax.axis_size("hour")
    own_block = whiten(spectra, quality)
    cos_t, neg_sin_t = lag_table(n_freq, hours * n_hour)

    others = (plan != 1) & (plan != n_chan - 1)
    low_mask = jnp.min(jnp.where(others, plan, n_chan))
    high_mask = jnp.max(jnp.where(others, plan, 0))
    branches = [
        (lambda v, m=m: xor_permute(v, "chan", m)) for m in range(1, n_chan)
    ]
    paired = [
        (lambda v, m=m: (xor_permute(v, "chan", n_chan - 1), xor_permute(v, "chan", m)))
        for m in range(1, n_chan)
    ]
    far_partner, low_partner = lax.switch(low_mask - 1, paired, own_block)
    partners = [
        xor_permute(own_block, "chan", 1),
        far_partner,
        low_partner,
        lax.switch(high_mask - 1, branches, own_block),
    ]
    re_parts, im_parts = [], []
    for partner in partners:
        cross_re, cross_im = cross_spectrum(own_block, partner)
        re_parts.append(cross_re)
        im_parts.append(cross_im)
    cross_re = jnp.stack(re_parts, axis=1).reshape(-1, n_freq)
    cross_im = jnp.stack(im_parts, axis=1).reshape(-1, n_freq)
    hp = lax.Precision.HIGH
    lagged = jnp.dot(cross_re, cos_t, precision=hp, preferred_element_type=jnp.float32)
    lagged = lagged + jnp.dot(
        cross_im, neg_sin_t, precision=hp, preferred_element_type=jnp.float32
    )
    lagged = lagged.reshape(chans, ROUNDS * chans, LAGS)

    gathered = lax.all_to_all(lagged, "hour", 0, 0, tiled=True)
    total = jnp.sum(gathered, axis=0).reshape(ROUNDS, chans, LAGS)

    slot = jnp.where(
        plan == 1,
        0,
        jnp.where(
            plan == n_chan - 1,
            1,
            jnp.where(plan == low_mask, 2, 3),
        ),
    ).astype(jnp.int32)
    result = jnp.take(total, slot, axis=0)
    return result[:, None]


def solution(mesh):
    return jax.shard_map(
        per_device,
        mesh=mesh,
        in_specs=(P("hour", "chan", None), P("chan"), P()),
        out_specs=P(None, "hour", "chan", None),
        check_vma=False,
    )
```

```python
import jax
import jax.numpy as jnp
from jax import lax
from jax.sharding import PartitionSpec as P

BAND = 64
LAGS = 512
ROUNDS = 4


def xor_permute(value, axis, mask):
    return lax.ppermute(value, axis, [(i, i ^ mask) for i in range(lax.axis_size(axis))])


def whiten(spectra, quality):
    hours, chans, width = spectra.shape
    n_freq = width // 2
    values = spectra.astype(jnp.float32)
    real_part = values[..., :n_freq]
    imag_part = values[..., n_freq:]
    power_sum = real_part * real_part + imag_part * imag_part
    band_mean = jnp.mean(
        power_sum.reshape(hours, chans, n_freq // BAND, BAND), axis=-1, keepdims=True
    )
    gain_band = lax.rsqrt(band_mean + 1e-06)
    gain_full = jnp.broadcast_to(gain_band, (hours, chans, n_freq // BAND, BAND)).reshape(
        hours, chans, n_freq
    )
    gain_both = jnp.concatenate([gain_full, gain_full], axis=-1)
    scaled = values * gain_both * quality.astype(jnp.float32)[None, :, None]
    return scaled.astype(jnp.bfloat16)


def lag_table(n_freq, total_hours):
    period = 2 * n_freq
    fine_n = 64
    lag_index = jnp.arange(LAGS, dtype=jnp.int32)[None, :] - LAGS // 2

    def angles(freqs):
        phase_int = freqs[:, None] * lag_index % period
        return jnp.pi * phase_int.astype(jnp.float32) / n_freq

    hi = angles(jnp.arange(n_freq // fine_n, dtype=jnp.int32) * fine_n)
    lo = angles(jnp.arange(fine_n, dtype=jnp.int32))
    cos_hi, sin_hi = jnp.cos(hi)[:, None, :], jnp.sin(hi)[:, None, :]
    cos_lo, sin_lo = jnp.cos(lo)[None, :, :], jnp.sin(lo)[None, :, :]
    factor = 1.0 / jnp.sqrt(jnp.float32(total_hours * n_freq))
    cos_t = (cos_hi * cos_lo - sin_hi * sin_lo).reshape(n_freq, LAGS) * factor
    neg_sin_t = (-(sin_hi * cos_lo + cos_hi * sin_lo)).reshape(n_freq, LAGS) * factor
    return cos_t, neg_sin_t


def cross_spectrum(own_block, partner):
    n_freq = own_block.shape[2] // 2
    a = own_block.astype(jnp.float32)
    b = partner.astype(jnp.float32)
    a_re = a[:, None, :, :n_freq]
    a_im = a[:, None, :, n_freq:]
    b_re = b[:, :, None, :n_freq]
    b_im = b[:, :, None, n_freq:]
    cross_re = jnp.sum(b_re * a_re + b_im * a_im, axis=0)
    cross_im = jnp.sum(b_re * a_im - b_im * a_re, axis=0)
    return cross_re, cross_im


def per_device(spectra, quality, plan):
    hours, chans, width = spectra.shape
    n_freq = width // 2
    n_chan = lax.axis_size("chan")
    n_hour = lax.axis_size("hour")
    own_block = whiten(spectra, quality)
    cos_t, neg_sin_t = lag_table(n_freq, hours * n_hour)

    others = (plan != 1) & (plan != n_chan - 1)
    low_mask = jnp.min(jnp.where(others, plan, n_chan))
    high_mask = jnp.max(jnp.where(others, plan, 0))
    branches = [
        (lambda v, m=m: xor_permute(v, "chan", m)) for m in range(1, n_chan)
    ]
    hp = lax.Precision.HIGH

    def lags_of(partners):
        re_parts, im_parts = [], []
        for partner in partners:
            cross_re, cross_im = cross_spectrum(own_block, partner)
            re_parts.append(cross_re)
            im_parts.append(cross_im)
        cross_re = jnp.stack(re_parts, axis=1).reshape(-1, n_freq)
        cross_im = jnp.stack(im_parts, axis=1).reshape(-1, n_freq)
        lagged = jnp.dot(cross_re, cos_t, precision=hp, preferred_element_type=jnp.float32)
        lagged = lagged + jnp.dot(
            cross_im, neg_sin_t, precision=hp, preferred_element_type=jnp.float32
        )
        return lagged.reshape(chans, len(partners) * chans, LAGS)

    def hour_sum(lagged):
        gathered = lax.all_to_all(lagged, "hour", 0, 0, tiled=True)
        return jnp.sum(gathered, axis=0)

    early = lags_of([
        xor_permute(own_block, "chan", 1),
        xor_permute(own_block, "chan", n_chan - 1),
        lax.switch(low_mask - 1, branches, own_block),
    ])
    fetch_and_sum = [
        (lambda v, e, m=m: (xor_permute(v, "chan", m), hour_sum(e)))
        for m in range(1, n_chan)
    ]
    high_partner, early_sum = lax.switch(high_mask - 1, fetch_and_sum, own_block, early)
    late_sum = hour_sum(lags_of([high_partner]))
    total = jnp.concatenate([early_sum, late_sum], axis=0).reshape(ROUNDS, chans, LAGS)

    slot = jnp.where(
        plan == 1,
        0,
        jnp.where(
            plan == n_chan - 1,
            1,
            jnp.where(plan == low_mask, 2, 3),
        ),
    ).astype(jnp.int32)
    result = jnp.take(total, slot, axis=0)
    return result[:, None]


def solution(mesh):
    return jax.shard_map(
        per_device,
        mesh=mesh,
        in_specs=(P("hour", "chan", None), P("chan"), P()),
        out_specs=P(None, "hour", "chan", None),
        check_vma=False,
    )
```

```python
import jax
import jax.numpy as jnp
from jax import lax
from jax.sharding import PartitionSpec as P

BAND = 64
LAGS = 512
ROUNDS = 4


def xor_permute(value, axis, mask):
    return lax.ppermute(value, axis, [(i, i ^ mask) for i in range(lax.axis_size(axis))])


def whiten(spectra, quality):
    hours, chans, width = spectra.shape
    n_freq = width // 2
    values = spectra.astype(jnp.float32)
    real_part = values[..., :n_freq]
    imag_part = values[..., n_freq:]
    power_sum = real_part * real_part + imag_part * imag_part
    band_mean = jnp.mean(
        power_sum.reshape(hours, chans, n_freq // BAND, BAND), axis=-1, keepdims=True
    )
    gain_band = lax.rsqrt(band_mean + 1e-06)
    gain_full = jnp.broadcast_to(gain_band, (hours, chans, n_freq // BAND, BAND)).reshape(
        hours, chans, n_freq
    )
    gain_both = jnp.concatenate([gain_full, gain_full], axis=-1)
    scaled = values * gain_both * quality.astype(jnp.float32)[None, :, None]
    return scaled.astype(jnp.bfloat16)


def lag_table(n_freq, total_hours):
    period = 2 * n_freq
    fine_n = 64
    lag_index = jnp.arange(1, LAGS // 2 + 1, dtype=jnp.int32)[None, :]

    def angles(freqs):
        phase_int = freqs[:, None] * lag_index % period
        return jnp.pi * phase_int.astype(jnp.float32) / n_freq

    hi = angles(jnp.arange(n_freq // fine_n, dtype=jnp.int32) * fine_n)
    lo = angles(jnp.arange(fine_n, dtype=jnp.int32))
    cos_hi, sin_hi = jnp.cos(hi)[:, None, :], jnp.sin(hi)[:, None, :]
    cos_lo, sin_lo = jnp.cos(lo)[None, :, :], jnp.sin(lo)[None, :, :]
    factor = 1.0 / jnp.sqrt(jnp.float32(total_hours * n_freq))
    cos_t = (cos_hi * cos_lo - sin_hi * sin_lo).reshape(n_freq, LAGS // 2) * factor
    sin_t = (sin_hi * cos_lo + cos_hi * sin_lo).reshape(n_freq, LAGS // 2) * factor
    return cos_t, sin_t, factor


def cross_spectrum(own_block, partner):
    n_freq = own_block.shape[2] // 2
    a = own_block.astype(jnp.float32)
    b = partner.astype(jnp.float32)
    a_re = a[:, None, :, :n_freq]
    a_im = a[:, None, :, n_freq:]
    b_re = b[:, :, None, :n_freq]
    b_im = b[:, :, None, n_freq:]
    cross_re = jnp.sum(b_re * a_re + b_im * a_im, axis=0)
    cross_im = jnp.sum(b_re * a_im - b_im * a_re, axis=0)
    return cross_re, cross_im


def per_device(spectra, quality, plan):
    hours, chans, width = spectra.shape
    n_freq = width // 2
    n_chan = lax.axis_size("chan")
    n_hour = lax.axis_size("hour")
    own_block = whiten(spectra, quality)
    cos_t, sin_t, factor = lag_table(n_freq, hours * n_hour)

    others = (plan != 1) & (plan != n_chan - 1)
    low_mask = jnp.min(jnp.where(others, plan, n_chan))
    high_mask = jnp.max(jnp.where(others, plan, 0))
    branches = [
        (lambda v, m=m: xor_permute(v, "chan", m)) for m in range(1, n_chan)
    ]
    partners = [
        xor_permute(own_block, "chan", 1),
        xor_permute(own_block, "chan", n_chan - 1),
        lax.switch(low_mask - 1, branches, own_block),
        lax.switch(high_mask - 1, branches, own_block),
    ]
    re_parts, im_parts = [], []
    for partner in partners:
        cross_re, cross_im = cross_spectrum(own_block, partner)
        re_parts.append(cross_re)
        im_parts.append(cross_im)
    cross_re = jnp.stack(re_parts, axis=1).reshape(-1, n_freq)
    cross_im = jnp.stack(im_parts, axis=1).reshape(-1, n_freq)
    hp = lax.Precision.HIGH
    even = jnp.dot(cross_re, cos_t, precision=hp, preferred_element_type=jnp.float32)
    odd = jnp.dot(cross_im, sin_t, precision=hp, preferred_element_type=jnp.float32)
    lagged = jnp.concatenate(
        [
            jnp.flip(even + odd, axis=1),
            jnp.sum(cross_re, axis=1, keepdims=True) * factor,
            (even - odd)[:, : LAGS // 2 - 1],
        ],
        axis=1,
    )
    lagged = lagged.reshape(chans, ROUNDS * chans, LAGS)

    gathered = lax.all_to_all(lagged, "hour", 0, 0, tiled=True)
    total = jnp.sum(gathered, axis=0).reshape(ROUNDS, chans, LAGS)

    slot = jnp.where(
        plan == 1,
        0,
        jnp.where(
            plan == n_chan - 1,
            1,
            jnp.where(plan == low_mask, 2, 3),
        ),
    ).astype(jnp.int32)
    result = jnp.take(total, slot, axis=0)
    return result[:, None]


def solution(mesh):
    return jax.shard_map(
        per_device,
        mesh=mesh,
        in_specs=(P("hour", "chan", None), P("chan"), P()),
        out_specs=P(None, "hour", "chan", None),
        check_vma=False,
    )
```

```python
import jax
import jax.numpy as jnp
from jax import lax
from jax.sharding import PartitionSpec as P

BAND = 64
LAGS = 512
ROUNDS = 4


def xor_permute(value, axis, mask):
    return lax.ppermute(value, axis, [(i, i ^ mask) for i in range(lax.axis_size(axis))])


def whiten(spectra, quality):
    hours, chans, width = spectra.shape
    n_freq = width // 2
    values = spectra.astype(jnp.float32)
    real_part = values[..., :n_freq]
    imag_part = values[..., n_freq:]
    power_sum = real_part * real_part + imag_part * imag_part
    band_mean = jnp.mean(
        power_sum.reshape(hours, chans, n_freq // BAND, BAND), axis=-1, keepdims=True
    )
    gain_band = lax.rsqrt(band_mean + 1e-06)
    gain_full = jnp.broadcast_to(gain_band, (hours, chans, n_freq // BAND, BAND)).reshape(
        hours, chans, n_freq
    )
    gain_both = jnp.concatenate([gain_full, gain_full], axis=-1)
    scaled = values * gain_both * quality.astype(jnp.float32)[None, :, None]
    return scaled.astype(jnp.bfloat16)


def lag_table(n_freq, total_hours):
    period = 2 * n_freq
    fine_n = 64
    lag_index = jnp.arange(1, LAGS // 2 + 1, dtype=jnp.int32)[None, :]

    def angles(freqs):
        phase_int = freqs[:, None] * lag_index % period
        return jnp.pi * phase_int.astype(jnp.float32) / n_freq

    hi = angles(jnp.arange(n_freq // fine_n, dtype=jnp.int32) * fine_n)
    lo = angles(jnp.arange(fine_n, dtype=jnp.int32))
    cos_hi, sin_hi = jnp.cos(hi)[:, None, :], jnp.sin(hi)[:, None, :]
    cos_lo, sin_lo = jnp.cos(lo)[None, :, :], jnp.sin(lo)[None, :, :]
    factor = 1.0 / jnp.sqrt(jnp.float32(total_hours * n_freq))
    cos_t = (cos_hi * cos_lo - sin_hi * sin_lo).reshape(n_freq, LAGS // 2) * factor
    sin_t = (sin_hi * cos_lo + cos_hi * sin_lo).reshape(n_freq, LAGS // 2) * factor
    return cos_t, sin_t, factor


def cross_spectrum(own_block, partner):
    n_freq = own_block.shape[2] // 2
    a = own_block.astype(jnp.float32)
    b = partner.astype(jnp.float32)
    a_re = a[:, None, :, :n_freq]
    a_im = a[:, None, :, n_freq:]
    b_re = b[:, :, None, :n_freq]
    b_im = b[:, :, None, n_freq:]
    cross_re = jnp.sum(b_re * a_re + b_im * a_im, axis=0)
    cross_im = jnp.sum(b_re * a_im - b_im * a_re, axis=0)
    return cross_re, cross_im


def per_device(spectra, quality, plan):
    hours, chans, width = spectra.shape
    n_freq = width // 2
    n_chan = lax.axis_size("chan")
    n_hour = lax.axis_size("hour")
    own_block = whiten(spectra, quality)
    cos_t, sin_t, factor = lag_table(n_freq, hours * n_hour)

    others = (plan != 1) & (plan != n_chan - 1)
    low_mask = jnp.min(jnp.where(others, plan, n_chan))
    high_mask = jnp.max(jnp.where(others, plan, 0))
    branches = [
        (lambda v, m=m: xor_permute(v, "chan", m)) for m in range(1, n_chan)
    ]
    partners = [
        xor_permute(own_block, "chan", 1),
        xor_permute(own_block, "chan", n_chan - 1),
        lax.switch(low_mask - 1, branches, own_block),
        lax.switch(high_mask - 1, branches, own_block),
    ]
    re_parts, im_parts = [], []
    for partner in partners:
        cross_re, cross_im = cross_spectrum(own_block, partner)
        re_parts.append(cross_re)
        im_parts.append(cross_im)
    cross_re = jnp.stack(re_parts, axis=1).reshape(-1, n_freq)
    cross_im = jnp.stack(im_parts, axis=1).reshape(-1, n_freq)
    hp = lax.Precision.HIGH
    even = jnp.dot(cross_re, cos_t, precision=hp, preferred_element_type=jnp.float32)
    odd = jnp.dot(cross_im, sin_t, precision=hp, preferred_element_type=jnp.float32)
    lagged = jnp.concatenate(
        [
            jnp.flip(even + odd, axis=1),
            jnp.sum(cross_re, axis=1, keepdims=True) * factor,
            (even - odd)[:, : LAGS // 2 - 1],
        ],
        axis=1,
    )
    lagged = lagged.reshape(chans, ROUNDS * chans, LAGS)

    gathered = lax.all_to_all(lagged, "hour", 0, 0, tiled=True)
    total = jnp.sum(gathered, axis=0).reshape(ROUNDS, chans, LAGS)

    slot = jnp.where(
        plan == 1,
        0,
        jnp.where(
            plan == n_chan - 1,
            1,
            jnp.where(plan == low_mask, 2, 3),
        ),
    ).astype(jnp.int32)
    pick = slot[:, None, None]
    result = jnp.where(
        pick == 0,
        total[0],
        jnp.where(pick == 1, total[1], jnp.where(pick == 2, total[2], total[3])),
    )
    return result[:, None]


def solution(mesh):
    return jax.shard_map(
        per_device,
        mesh=mesh,
        in_specs=(P("hour", "chan", None), P("chan"), P()),
        out_specs=P(None, "hour", "chan", None),
        check_vma=False,
    )
```

```python
import jax
import jax.numpy as jnp
from jax import lax
from jax.sharding import PartitionSpec as P

BAND = 64
LAGS = 512
ROUNDS = 4


def xor_permute(value, axis, mask):
    return lax.ppermute(value, axis, [(i, i ^ mask) for i in range(lax.axis_size(axis))])


def whiten(spectra, quality):
    hours, chans, width = spectra.shape
    n_freq = width // 2
    lanes = 128
    values = spectra.astype(jnp.float32)
    real_part = values[..., :n_freq]
    imag_part = values[..., n_freq:]
    power_sum = (real_part * real_part + imag_part * imag_part).reshape(-1, lanes)
    lane = jnp.arange(lanes, dtype=jnp.int32)
    select = (lane[:, None] // BAND == jnp.arange(lanes // BAND)[None, :]).astype(jnp.float32)
    band_sum = jnp.dot(power_sum, select, precision=lax.Precision.HIGHEST)
    gain_band = lax.rsqrt(band_sum / BAND + 1e-06)
    gain_full = jnp.dot(gain_band, select.T, precision=lax.Precision.HIGHEST)
    gain_full = gain_full.reshape(hours, chans, n_freq)
    gain_both = jnp.concatenate([gain_full, gain_full], axis=-1)
    scaled = values * gain_both * quality.astype(jnp.float32)[None, :, None]
    return scaled.astype(jnp.bfloat16)


def lag_table(n_freq, total_hours):
    period = 2 * n_freq
    fine_n = 64
    lag_index = jnp.arange(1, LAGS // 2 + 1, dtype=jnp.int32)[None, :]

    def angles(freqs):
        phase_int = freqs[:, None] * lag_index % period
        return jnp.pi * phase_int.astype(jnp.float32) / n_freq

    hi = angles(jnp.arange(n_freq // fine_n, dtype=jnp.int32) * fine_n)
    lo = angles(jnp.arange(fine_n, dtype=jnp.int32))
    cos_hi, sin_hi = jnp.cos(hi)[:, None, :], jnp.sin(hi)[:, None, :]
    cos_lo, sin_lo = jnp.cos(lo)[None, :, :], jnp.sin(lo)[None, :, :]
    factor = 1.0 / jnp.sqrt(jnp.float32(total_hours * n_freq))
    cos_t = (cos_hi * cos_lo - sin_hi * sin_lo).reshape(n_freq, LAGS // 2) * factor
    sin_t = (sin_hi * cos_lo + cos_hi * sin_lo).reshape(n_freq, LAGS // 2) * factor
    return cos_t, sin_t, factor


def cross_spectrum(own_block, partner):
    n_freq = own_block.shape[2] // 2
    a = own_block.astype(jnp.float32)
    b = partner.astype(jnp.float32)
    a_re = a[:, None, :, :n_freq]
    a_im = a[:, None, :, n_freq:]
    b_re = b[:, :, None, :n_freq]
    b_im = b[:, :, None, n_freq:]
    cross_re = jnp.sum(b_re * a_re + b_im * a_im, axis=0)
    cross_im = jnp.sum(b_re * a_im - b_im * a_re, axis=0)
    return cross_re, cross_im


def per_device(spectra, quality, plan):
    hours, chans, width = spectra.shape
    n_freq = width // 2
    n_chan = lax.axis_size("chan")
    n_hour = lax.axis_size("hour")
    own_block = whiten(spectra, quality)
    cos_t, sin_t, factor = lag_table(n_freq, hours * n_hour)

    others = (plan != 1) & (plan != n_chan - 1)
    low_mask = jnp.min(jnp.where(others, plan, n_chan))
    high_mask = jnp.max(jnp.where(others, plan, 0))
    branches = [
        (lambda v, m=m: xor_permute(v, "chan", m)) for m in range(1, n_chan)
    ]
    partners = [
        xor_permute(own_block, "chan", 1),
        xor_permute(own_block, "chan", n_chan - 1),
        lax.switch(low_mask - 1, branches, own_block),
        lax.switch(high_mask - 1, branches, own_block),
    ]
    re_parts, im_parts = [], []
    for partner in partners:
        cross_re, cross_im = cross_spectrum(own_block, partner)
        re_parts.append(cross_re)
        im_parts.append(cross_im)
    cross_re = jnp.stack(re_parts, axis=1).reshape(-1, n_freq)
    cross_im = jnp.stack(im_parts, axis=1).reshape(-1, n_freq)
    hp = lax.Precision.HIGH
    even = jnp.dot(cross_re, cos_t, precision=hp, preferred_element_type=jnp.float32)
    odd = jnp.dot(cross_im, sin_t, precision=hp, preferred_element_type=jnp.float32)
    lagged = jnp.concatenate(
        [
            even + odd,
            jnp.sum(cross_re, axis=1, keepdims=True) * factor,
            (even - odd)[:, : LAGS // 2 - 1],
        ],
        axis=1,
    )
    lagged = lagged.reshape(chans, ROUNDS * chans, LAGS)

    gathered = lax.all_to_all(lagged, "hour", 0, 0, tiled=True)
    total = jnp.sum(gathered, axis=0).reshape(ROUNDS, chans, LAGS)

    slot = jnp.where(
        plan == 1,
        0,
        jnp.where(
            plan == n_chan - 1,
            1,
            jnp.where(plan == low_mask, 2, 3),
        ),
    ).astype(jnp.int32)
    pick = slot[:, None, None]
    result = jnp.where(
        pick == 0,
        total[0],
        jnp.where(pick == 1, total[1], jnp.where(pick == 2, total[2], total[3])),
    )
    result = jnp.concatenate(
        [jnp.flip(result[..., : LAGS // 2], axis=-1), result[..., LAGS // 2 :]], axis=-1
    )
    return result[:, None]


def solution(mesh):
    return jax.shard_map(
        per_device,
        mesh=mesh,
        in_specs=(P("hour", "chan", None), P("chan"), P()),
        out_specs=P(None, "hour", "chan", None),
        check_vma=False,
    )
```
